512 devices in a mesh: dp: 32 (over y, z_hi), seq: 16 (over x, z_lo, core).
Axes of the slice: x: 4, y: 8, z: 8 (z_hi: 4, z_lo: 2; z = z_hi * 2 + z_lo), core: 2. Of those that a mesh axis runs over, the one named last changes fastest.
Arguments:
- queries: bfloat16 [32, 2048, 1024], P('dp', 'seq'), may hold values from -6 to 6
- key_input: bfloat16 [32, 2048, 1024], P('dp', 'seq'), may hold values from -6 to 6
- values: bfloat16 [32, 2048, 1024], P('dp', 'seq'), may hold values from -6 to 6
- cotangent: bfloat16 [32, 2048, 1024], P('dp', 'seq'), may hold values from -12 to 12
- tile_mask: int32 [32, 32, 32], P('dp'), may hold values from 0 to 1, as said below
- condition_flags: int32 [32, 2048], P('dp', 'seq'), may hold values 0 or 1
- condition_embed: float32 [2, 1024], replicated, may hold values from -4 to 4
Outputs:
- attended: bfloat16 [32, 2048, 1024], P('dp', 'seq')
- grad_queries: bfloat16 [32, 2048, 1024], P('dp', 'seq')
- grad_keys: bfloat16 [32, 2048, 1024], P('dp', 'seq')
- grad_values: bfloat16 [32, 2048, 1024], P('dp', 'seq')
- grad_condition: float32 [2, 1024], replicated
The draws below stay inside these ranges and needn't reach their ends.
Inputs may be any that keep to these rules, and one draw needn't show every extreme that they name: tile_mask[b, i, i] is 1; tile_mask[b, i, j] is 0 unless j < 2 or the absolute difference of i // 2 and j // 2 is at most 1.
All inputs are finite; a program needn't handle non-finite values. No bound on the sum of `condition_flags` on one device may be relied on, other than what follows from the above.
Results may differ from the reference program's by a relative error of at most 0.008.
The reference program's roundings to bfloat16 on the way count: a program that leaves them out, or rounds other values in their place, can miss the bound.
Values may be sent and summed in bfloat16 or wider, within the bound.
No kernel may reach another device: no remote copies, remote signals or barrier semaphores. Data moves between devices by JAX's collectives and lax.ppermute only.
A program may use at most 64 MiB of HBM per device.

```python
import math
import jax
import jax.numpy as jnp
from jax import lax

HEADS = 8
HEAD_DIM = 128
BLOCK = 64
ATTN_WIDTH = 1024
SEQ_LEN = 2048
DEV_BLOCKS = 2
SEQ_BLOCKS = 32
BATCH = 32


def draw_queries(key, part):
    result = jnp.clip(jax.random.normal(jax.random.fold_in(key, 1), (BATCH, SEQ_LEN, ATTN_WIDTH), jnp.float32), -6.0, 6.0)
    return result.astype(jnp.bfloat16)


def draw_key_input(key, part):
    result = jnp.clip(jax.random.normal(jax.random.fold_in(key, 2), (BATCH, SEQ_LEN, ATTN_WIDTH), jnp.float32), -6.0, 6.0)
    return result.astype(jnp.bfloat16)


def draw_tile_mask(key, part):
    tile_rows = jnp.arange(SEQ_BLOCKS)
    owner = tile_rows // DEV_BLOCKS
    reachable = (jnp.abs(owner[:, None] - owner[None, :]) <= 1) | (owner[None, :] == 0)
    coin = jax.random.randint(jax.random.fold_in(key, 3), (BATCH, SEQ_BLOCKS, SEQ_BLOCKS), 0, 5) < 3
    diagonal = tile_rows[:, None] == tile_rows[None, :]
    return jnp.where(diagonal[None] | reachable[None] & coin, 1, 0).astype(jnp.int32)


def set_ends(entries, rng, least, high):
    extent = entries.shape
    place = [jax.random.randint(jax.random.fold_in(rng, axis), (), 0, extent[axis]) for axis in range(len(extent))]
    entries = entries.at[tuple(place)].set(least)
    longest = extent.index(max(extent))
    place[longest] = (place[longest] + 1) % extent[longest]
    return entries.at[tuple(place)].set(high)


def block_levels(own_key, shape, shards, smallest, largest):
    level = 1.0
    for dim, parts in shards:
        steps = jax.random.uniform(jax.random.fold_in(jax.random.fold_in(own_key, 6), dim), (parts,), jnp.float32, smallest / len(shards), largest / len(shards))
        level = level * jnp.repeat(jnp.exp(steps), shape[dim] // parts).reshape((-1,) + (1,) * (len(shape) - 1 - dim))
    return level


def normal_values(own_key, extent, deviation, limit, shards=(), dtype=jnp.bfloat16):
    entries = jax.random.normal(own_key, extent, jnp.float32) * deviation
    if len(shards) > 0:
        entries = block_levels(own_key, extent, shards, -0.22, 0.18) * entries
    return jnp.clip(entries, min=-limit, max=limit).astype(dtype)


def setup_inputs(seed: int = 0) -> dict:
    key_list = jax.random.split(jax.random.key(seed), 8)
    queries = draw_queries(jax.random.fold_in(key_list[7], 71), 0)
    key_input = draw_key_input(jax.random.fold_in(key_list[7], 71), 0)
    values = normal_values(key_list[2], (BATCH, SEQ_LEN, ATTN_WIDTH), 1.0, 6.0, ((0, 32), (1, 16)))
    cotangent = normal_values(key_list[3], (BATCH, SEQ_LEN, ATTN_WIDTH), 2.0, 12.0, ((0, 32), (1, 16)))
    tile_mask = draw_tile_mask(jax.random.fold_in(key_list[7], 71), 0)
    condition_flags = set_ends((jax.random.randint(key_list[5], (BATCH, SEQ_LEN), 0, 2) < 1).astype(jnp.int32), jax.random.fold_in(key_list[5], 1), 0, 1)
    condition_embed = normal_values(key_list[6], (2, ATTN_WIDTH), 0.7, 4.0, (), jnp.float32)
    return {"queries": queries, "key_input": key_input, "values": values, "cotangent": cotangent, "tile_mask": tile_mask, "condition_flags": condition_flags, "condition_embed": condition_embed}


masked_score = -1e+30

def contract_last(left, right):
    return lax.dot_general(left, right, (((1,), (1,)), ((), ())), preferred_element_type=jnp.float32)

def contract_first(left, right):
    return lax.dot_general(left, right, (((0,), (0,)), ((), ())), preferred_element_type=jnp.float32)

def reference(queries, key_input, values, cotangent, tile_mask, condition_flags, condition_embed):
    score_scale = 1.0 / math.sqrt(HEAD_DIM)

    def one_graph(arrays):
        query_rows, key_rows, value_rows, grad_rows, tiles, flags = arrays
        flag_column = flags.astype(jnp.float32)[:, None]
        query_eff = (query_rows.astype(jnp.float32) + flag_column * condition_embed[0][None, :]).astype(jnp.bfloat16)
        key_eff = (key_rows.astype(jnp.float32) + flag_column * condition_embed[1][None, :]).astype(jnp.bfloat16)
        allowed = jnp.repeat(jnp.repeat(tiles, BLOCK, axis=0), BLOCK, axis=1) > 0
        outputs = []
        log_list = []
        for head in range(HEADS):
            first_col = head * HEAD_DIM
            last_col = first_col + HEAD_DIM
            scores = jnp.where(allowed, contract_last(query_eff[:, first_col:last_col], key_eff[:, first_col:last_col]) * score_scale, masked_score)
            top = lax.optimization_barrier(jnp.max(scores, axis=1, keepdims=True))
            total = lax.optimization_barrier(jnp.sum(jnp.where(allowed, jnp.exp(scores - top), 0.0), axis=1, keepdims=True))
            log_total = top + jnp.log(total)
            weights = jnp.where(allowed, jnp.exp(scores - log_total), 0.0)
            outputs.append(jnp.dot(weights.astype(jnp.bfloat16), value_rows[:, first_col:last_col], preferred_element_type=jnp.float32))
            log_list.append(log_total)
        attended = jnp.concatenate(outputs, axis=1).astype(jnp.bfloat16)
        deltas = lax.optimization_barrier(jnp.sum((grad_rows.astype(jnp.float32) * attended.astype(jnp.float32)).reshape(SEQ_LEN, HEADS, HEAD_DIM), axis=2))
        query_grads = []
        key_grads = []
        value_grads = []
        for head in range(HEADS):
            first_col = head * HEAD_DIM
            last_col = first_col + HEAD_DIM
            scores = jnp.where(allowed, contract_last(query_eff[:, first_col:last_col], key_eff[:, first_col:last_col]) * score_scale, masked_score)
            weights = jnp.where(allowed, jnp.exp(scores - log_list[head]), 0.0)
            dprob = contract_last(grad_rows[:, first_col:last_col], value_rows[:, first_col:last_col])
            dscore = (weights * (dprob - deltas[:, head:head + 1]) * score_scale).astype(jnp.bfloat16)
            query_grads.append(jnp.dot(dscore, key_eff[:, first_col:last_col], preferred_element_type=jnp.float32))
            key_grads.append(contract_first(dscore, query_eff[:, first_col:last_col]))
            value_grads.append(contract_first(weights.astype(jnp.bfloat16), grad_rows[:, first_col:last_col]))
        qsum = jnp.concatenate(query_grads, axis=1)
        ksum = jnp.concatenate(key_grads, axis=1)
        vsum = jnp.concatenate(value_grads, axis=1)
        cond_rows = jnp.stack([lax.optimization_barrier(jnp.sum(flag_column * qsum, axis=0)), lax.optimization_barrier(jnp.sum(flag_column * ksum, axis=0))])
        return (attended, qsum.astype(jnp.bfloat16), ksum.astype(jnp.bfloat16), vsum.astype(jnp.bfloat16), cond_rows)
    attended, grad_queries, grad_keys, grad_values, cond_rows = lax.map(one_graph, (queries, key_input, values, cotangent, tile_mask, condition_flags))
    grad_condition = lax.optimization_barrier(jnp.sum(cond_rows, axis=0)) / BATCH
    return (attended, grad_queries, grad_keys, grad_values, grad_condition)
```

```python
import math

import jax
import jax.numpy as jnp
import numpy as np
from jax import lax
from jax.sharding import PartitionSpec as P

HEAD_DIM = 128
BLOCK = 64


masked_score = -1e30


def broadcast_stages(count):
    if count == 16:
        return [
            [[(0, 2)], [(0, 4)], [(0, 8)], [(0, 12)]],
            [[(2, 3), (4, 5), (8, 9), (12, 13)], [(4, 6), (8, 10), (12, 14)], [(4, 7), (8, 11), (12, 15)]],
        ]
    stages = []
    have = 1
    while have < count:
        stages.append([[(i, i + have) for i in range(have) if i + have < count]])
        have *= 2
    return stages


def shift(x, step, count):
    if step > 0:
        pairs = [(i, i + step) for i in range(count - step)]
    else:
        pairs = [(i, i + step) for i in range(-step, count)]
    return lax.ppermute(x, "seq", pairs)


def tree_broadcast(block, seq_index, count):
    held = None
    source = block
    for stage in broadcast_stages(count):
        got = [lax.ppermute(source, "seq", pairs) for pairs in stage]
        stage_sum = got[0]
        for more in got[1:]:
            stage_sum = stage_sum + more
        held = stage_sum if held is None else held + stage_sum
        source = held if count == 16 else jnp.where(seq_index == 0, block, held)
    return held


def tree_reduce(part, count):
    total = part
    for stage in reversed(broadcast_stages(count)):
        incoming = [lax.ppermute(total, "seq", [(b, a) for a, b in pairs]) for pairs in stage]
        for got in incoming:
            total = total + got
    return total


def butterfly_sum(x, axis, count):
    step = 1
    while step < count:
        x = x + lax.ppermute(x, axis, [(i, i ^ step) for i in range(count)])
        step *= 2
    return x


def expand_tiles(tiles, block_rows):
    return jnp.repeat(jnp.repeat(tiles, block_rows, axis=0), block_rows, axis=1) > 0


def body(queries, key_input, values, cotangent, tile_mask, condition_flags, condition_embed):
    graph_count = queries.shape[0] * lax.axis_size("dp")
    dp_count = lax.axis_size("dp")
    seq_count = lax.axis_size("seq")
    seq_index = lax.axis_index("seq")
    query_rows = queries[0]
    key_rows = key_input[0]
    value_rows = values[0]
    grad_rows = cotangent[0]
    tok_rows, width = query_rows.shape
    head_dim = HEAD_DIM
    head_count = width // head_dim
    block_rows = BLOCK
    query_blocks = tok_rows // block_rows
    score_scale = 1.0 / math.sqrt(head_dim)

    flags = condition_flags[0]
    flag_column = flags.astype(jnp.float32)[:, None]
    query_eff = (query_rows.astype(jnp.float32) + flag_column * condition_embed[0][None, :]).astype(
        jnp.bfloat16
    )
    key_eff = (key_rows.astype(jnp.float32) + flag_column * condition_embed[1][None, :]).astype(
        jnp.bfloat16
    )

    flag_rows = jnp.zeros((16, width), jnp.bfloat16)
    flag_rows = lax.dynamic_update_slice(flag_rows, flags.astype(jnp.bfloat16)[None, :], (0, 0))
    own_pack = jnp.concatenate([key_eff, value_rows, flag_rows], axis=0)
    from_left = shift(own_pack, 1, seq_count)
    from_right = shift(own_pack, -1, seq_count)
    from_first = tree_broadcast(own_pack, seq_index, seq_count)
    slot_packs = [from_first, from_left, own_pack, from_right]

    tile_table = tile_mask[0]
    block_count = tile_table.shape[0]
    own_tiles = lax.dynamic_slice_in_dim(tile_table, seq_index * query_blocks, query_blocks, 0)
    slot_starts = [
        0,
        (seq_index - 1) * query_blocks,
        seq_index * query_blocks,
        (seq_index + 1) * query_blocks,
    ]
    slot_valid = [seq_index >= 2, seq_index >= 1, seq_index >= 0, seq_index <= seq_count - 2]
    slot_tiles = []
    for slot in range(4):
        start_block = jnp.clip(slot_starts[slot], 0, block_count - query_blocks)
        columns = lax.dynamic_slice_in_dim(own_tiles, start_block, query_blocks, 1)
        slot_tiles.append(jnp.where(slot_valid[slot], columns, 0))
    allowed = expand_tiles(jnp.concatenate(slot_tiles, axis=1), block_rows)

    key_set = jnp.concatenate([pack[:tok_rows] for pack in slot_packs], axis=0)
    value_set = jnp.concatenate([pack[tok_rows : 2 * tok_rows] for pack in slot_packs], axis=0)
    key_flags = jnp.concatenate(
        [pack[2 * tok_rows, :tok_rows] for pack in slot_packs], axis=0
    ).astype(jnp.float32)

    key_count = key_set.shape[0]
    q3 = query_eff.reshape(tok_rows, head_count, head_dim)
    g3 = grad_rows.reshape(tok_rows, head_count, head_dim)
    k3 = key_set.reshape(key_count, head_count, head_dim)
    v3 = value_set.reshape(key_count, head_count, head_dim)
    f32 = jnp.float32

    scores = jnp.where(
        allowed[None],
        jnp.einsum("qhd,khd->hqk", q3, k3, preferred_element_type=f32) * score_scale,
        masked_score,
    )
    top = jnp.max(scores, axis=2, keepdims=True)
    total = jnp.sum(jnp.where(allowed[None], jnp.exp(scores - top), 0.0), axis=2, keepdims=True)
    log_total = top + jnp.log(total)
    weights = jnp.where(allowed[None], jnp.exp(scores - log_total), 0.0)
    weights_half = weights.astype(jnp.bfloat16)
    attended = jnp.einsum("hqk,khd->qhd", weights_half, v3, preferred_element_type=f32).astype(
        jnp.bfloat16
    )
    delta = jnp.sum(g3.astype(f32) * attended.astype(f32), axis=2)
    dprob = jnp.einsum("qhd,khd->hqk", g3, v3, preferred_element_type=f32)
    dscore = (weights * (dprob - delta.T[:, :, None]) * score_scale).astype(jnp.bfloat16)
    query_total = jnp.einsum("hqk,khd->qhd", dscore, k3, preferred_element_type=f32).reshape(
        tok_rows, width
    )
    key_part = jnp.einsum("hqk,qhd->khd", dscore, q3, preferred_element_type=f32).reshape(
        key_count, width
    )
    value_part = jnp.einsum("hqk,qhd->khd", weights_half, g3, preferred_element_type=f32).reshape(
        key_count, width
    )

    cond_part = jnp.stack(
        [
            jnp.sum(jnp.where(flag_column > 0, query_total, 0.0), axis=0),
            jnp.sum(jnp.where(key_flags[:, None] > 0, key_part, 0.0), axis=0),
        ]
    )

    parts = [
        jnp.concatenate(
            [key_part[slot * tok_rows : (slot + 1) * tok_rows],
             value_part[slot * tok_rows : (slot + 1) * tok_rows]],
            axis=1,
        )
        for slot in range(4)
    ]
    back_from_right = shift(parts[1], -1, seq_count)
    back_from_left = shift(parts[3], 1, seq_count)
    first_total = tree_reduce(parts[0], seq_count)
    kv_total = parts[2] + back_from_right + back_from_left
    kv_total = kv_total + jnp.where(seq_index == 0, first_total, 0.0)

    cond_grad = butterfly_sum(butterfly_sum(cond_part, "seq", seq_count), "dp", dp_count)
    cond_grad = cond_grad / graph_count
    return (
        attended.reshape(tok_rows, width)[None],
        query_total.astype(jnp.bfloat16)[None],
        kv_total[:, :width].astype(jnp.bfloat16)[None],
        kv_total[:, width:].astype(jnp.bfloat16)[None],
        cond_grad,
    )


def solution(mesh):
    placed = (
        P("dp", "seq", None),
        P("dp", "seq", None),
        P("dp", "seq", None),
        P("dp", "seq", None),
        P("dp", None, None),
        P("dp", "seq"),
        P(),
    )
    return jax.shard_map(
        body,
        mesh=mesh,
        in_specs=placed,
        out_specs=(
            P("dp", "seq", None),
            P("dp", "seq", None),
            P("dp", "seq", None),
            P("dp", "seq", None),
            P(),
        ),
        check_vma=False,
    )
```

```python
import math

import jax
import jax.numpy as jnp
import numpy as np
from jax import lax
from jax.sharding import PartitionSpec as P

HEAD_DIM = 128
BLOCK = 64


masked_score = -1e30


def broadcast_stages(count):
    if count == 16:
        return [
            [[(0, 2)], [(0, 4)], [(0, 8)], [(0, 12)]],
            [[(2, 3), (4, 5), (8, 9), (12, 13)], [(4, 6), (8, 10), (12, 14)], [(4, 7), (8, 11), (12, 15)]],
        ]
    stages = []
    have = 1
    while have < count:
        stages.append([[(i, i + have) for i in range(have) if i + have < count]])
        have *= 2
    return stages


def shift(x, step, count):
    if step > 0:
        pairs = [(i, i + step) for i in range(count - step)]
    else:
        pairs = [(i, i + step) for i in range(-step, count)]
    return lax.ppermute(x, "seq", pairs)


def tree_broadcast(block, seq_index, count):
    held = None
    source = block
    for stage in broadcast_stages(count):
        got = [lax.ppermute(source, "seq", pairs) for pairs in stage]
        stage_sum = got[0]
        for more in got[1:]:
            stage_sum = stage_sum + more
        held = stage_sum if held is None else held + stage_sum
        source = held if count == 16 else jnp.where(seq_index == 0, block, held)
    return held


def tree_reduce(part, count):
    total = part
    for stage in reversed(broadcast_stages(count)):
        incoming = [lax.ppermute(total, "seq", [(b, a) for a, b in pairs]) for pairs in stage]
        for got in incoming:
            total = total + got
    return total


def butterfly_sum(x, axis, count):
    step = 1
    while step < count:
        x = x + lax.ppermute(x, axis, [(i, i ^ step) for i in range(count)])
        step *= 2
    return x


def expand_tiles(tiles, block_rows):
    return jnp.repeat(jnp.repeat(tiles, block_rows, axis=0), block_rows, axis=1) > 0


def body(queries, key_input, values, cotangent, tile_mask, condition_flags, condition_embed):
    graph_count = queries.shape[0] * lax.axis_size("dp")
    dp_count = lax.axis_size("dp")
    seq_count = lax.axis_size("seq")
    seq_index = lax.axis_index("seq")
    query_rows = queries[0]
    key_rows = key_input[0]
    value_rows = values[0]
    grad_rows = cotangent[0]
    tok_rows, width = query_rows.shape
    head_dim = HEAD_DIM
    head_count = width // head_dim
    block_rows = BLOCK
    query_blocks = tok_rows // block_rows
    score_scale = 1.0 / math.sqrt(head_dim)

    flags = condition_flags[0]
    flag_column = flags.astype(jnp.float32)[:, None]
    query_eff = (query_rows.astype(jnp.float32) + flag_column * condition_embed[0][None, :]).astype(
        jnp.bfloat16
    )
    key_eff = (key_rows.astype(jnp.float32) + flag_column * condition_embed[1][None, :]).astype(
        jnp.bfloat16
    )

    flag_rows = jnp.zeros((16, width), jnp.bfloat16)
    flag_rows = lax.dynamic_update_slice(flag_rows, flags.astype(jnp.bfloat16)[None, :], (0, 0))
    own_pack = jnp.concatenate([key_eff, value_rows, flag_rows], axis=0)
    from_left = shift(own_pack, 1, seq_count)
    from_right = shift(own_pack, -1, seq_count)
    from_first = tree_broadcast(own_pack, seq_index, seq_count)
    slot_packs = [from_first, from_left, own_pack, from_right]

    tile_table = tile_mask[0]
    block_count = tile_table.shape[0]
    own_tiles = lax.dynamic_slice_in_dim(tile_table, seq_index * query_blocks, query_blocks, 0)
    slot_starts = [
        0,
        (seq_index - 1) * query_blocks,
        seq_index * query_blocks,
        (seq_index + 1) * query_blocks,
    ]
    slot_valid = [seq_index >= 2, seq_index >= 1, seq_index >= 0, seq_index <= seq_count - 2]
    slot_tiles = []
    for slot in range(4):
        start_block = jnp.clip(slot_starts[slot], 0, block_count - query_blocks)
        columns = lax.dynamic_slice_in_dim(own_tiles, start_block, query_blocks, 1)
        slot_tiles.append(jnp.where(slot_valid[slot], columns, 0))
    allowed = expand_tiles(jnp.concatenate(slot_tiles, axis=1), block_rows)

    key_set = jnp.concatenate([pack[:tok_rows] for pack in slot_packs], axis=0)
    value_set = jnp.concatenate([pack[tok_rows : 2 * tok_rows] for pack in slot_packs], axis=0)
    key_flags = jnp.concatenate(
        [pack[2 * tok_rows, :tok_rows] for pack in slot_packs], axis=0
    ).astype(jnp.float32)

    key_count = key_set.shape[0]
    q3 = query_eff.reshape(tok_rows, head_count, head_dim)
    g3 = grad_rows.reshape(tok_rows, head_count, head_dim)
    k3 = key_set.reshape(key_count, head_count, head_dim)
    v3 = value_set.reshape(key_count, head_count, head_dim)
    f32 = jnp.float32

    scores = jnp.where(
        allowed[None],
        jnp.einsum("qhd,khd->hqk", q3, k3, preferred_element_type=f32) * score_scale,
        masked_score,
    )
    top = jnp.max(scores, axis=2, keepdims=True)
    total = jnp.sum(jnp.where(allowed[None], jnp.exp(scores - top), 0.0), axis=2, keepdims=True)
    log_total = top + jnp.log(total)
    weights = jnp.where(allowed[None], jnp.exp(scores - log_total), 0.0)
    weights_half = weights.astype(jnp.bfloat16)
    attended = jnp.einsum("hqk,khd->qhd", weights_half, v3, preferred_element_type=f32).astype(
        jnp.bfloat16
    )
    delta = jnp.sum(g3.astype(f32) * attended.astype(f32), axis=2)
    dprob = jnp.einsum("qhd,khd->hqk", g3, v3, preferred_element_type=f32)
    dscore = (weights * (dprob - delta.T[:, :, None]) * score_scale).astype(jnp.bfloat16)
    query_total = jnp.einsum("hqk,khd->qhd", dscore, k3, preferred_element_type=f32).reshape(
        tok_rows, width
    )
    pair_left = jnp.concatenate([dscore, weights_half], axis=0)
    pair_right = jnp.concatenate([q3, g3], axis=1)
    kv_part = jnp.einsum("hqk,qhd->khd", pair_left, pair_right, preferred_element_type=f32).reshape(
        key_count, 2 * width
    )
    key_part = kv_part[:, :width]

    cond_part = jnp.stack(
        [
            jnp.sum(jnp.where(flag_column > 0, query_total, 0.0), axis=0),
            jnp.sum(jnp.where(key_flags[:, None] > 0, key_part, 0.0), axis=0),
        ]
    )

    parts = [kv_part[slot * tok_rows : (slot + 1) * tok_rows] for slot in range(4)]
    back_from_right = shift(parts[1], -1, seq_count)
    back_from_left = shift(parts[3], 1, seq_count)
    first_total = tree_reduce(parts[0], seq_count)
    kv_total = parts[2] + back_from_right + back_from_left
    kv_total = kv_total + jnp.where(seq_index == 0, first_total, 0.0)

    cond_grad = butterfly_sum(butterfly_sum(cond_part, "dp", dp_count), "seq", seq_count)
    cond_grad = cond_grad / graph_count
    return (
        attended.reshape(tok_rows, width)[None],
        query_total.astype(jnp.bfloat16)[None],
        kv_total[:, :width].astype(jnp.bfloat16)[None],
        kv_total[:, width:].astype(jnp.bfloat16)[None],
        cond_grad,
    )


def solution(mesh):
    placed = (
        P("dp", "seq", None),
        P("dp", "seq", None),
        P("dp", "seq", None),
        P("dp", "seq", None),
        P("dp", None, None),
        P("dp", "seq"),
        P(),
    )
    return jax.shard_map(
        body,
        mesh=mesh,
        in_specs=placed,
        out_specs=(
            P("dp", "seq", None),
            P("dp", "seq", None),
            P("dp", "seq", None),
            P("dp", "seq", None),
            P(),
        ),
        check_vma=False,
    )
```
